512 devices in a mesh: expert: 64 (over z, y), tensor: 8 (over x, core).
Axes of the slice: x: 4, y: 8, z: 8, core: 2. Of those that a mesh axis runs over, the one named last changes fastest.
Arguments:
- hidden_rows: bfloat16 [2, 1024, 3584], P(None, 'expert', 'tensor'), may hold values from -6 to 6
- draft_len: int32 [2, 256], P(None, 'expert'), may hold values from 1 to 4, 640 in all within a row
- expert_ids: int32 [2, 1024, 8], P(None, 'expert'), may hold values from 0 to 55, all different within a row; in each aligned block of 16 rows (0 to 15, 16 to 31, ..., all dimensions but the last counted through in order) at most 4 rows name the same one
- replica: int32 [2, 1024, 8], P(None, 'expert'), may hold values from 0 to 1
- route_gain: float32 [2, 1024, 8], P(None, 'expert'), may hold values from 0.03 to 0.5
- slot_up: bfloat16 [64, 3584, 1024], P('expert', None, 'tensor'), may hold values from -0.09375 to 0.09375
- slot_down: bfloat16 [64, 1024, 3584], P('expert', 'tensor'), may hold values from -0.1875 to 0.1875
- shared_up: bfloat16 [3584, 1024], P(None, 'tensor'), may hold values from -0.09375 to 0.09375
- shared_down: bfloat16 [1024, 3584], P('tensor'), may hold values from -0.1875 to 0.1875
Outputs:
- mixed: bfloat16 [2, 1024, 3584], P(None, 'expert', 'tensor')
The draws below stay inside these ranges and needn't reach their ends.
Inputs may be any that keep to these rules, and one draw needn't show every extreme that they name: `expert_ids`: in each step, the 16 row places of one index of expert (live or not) name any one expert at most 4 times. Only the first 8 experts have a replica slot; for the other experts the value has no effect. `draft_len`: in each step the lengths of all 256 requests sum to 640.
All inputs are finite; a program needn't handle non-finite values. No bound on the sum of `draft_len` on one device may be relied on, other than what follows from the above.
Results may differ from the reference program's by a relative error of at most 0.019.
Values may be sent and summed in bfloat16 or wider, within the bound.
No kernel may reach another device: no remote copies, remote signals or barrier semaphores. Data moves between devices by JAX's collectives and lax.ppermute only.
A program may use at most 192 MiB of HBM per device.

```python
import math
import jax
import jax.numpy as jnp
import numpy as np
from jax import lax

D = 3584
H = 1024
HS = 1024
TOP = 8
SPAN = 4
STEPS = 2
H_PART = 128
ROWS_DEV = 16
REQUESTS = 256
ROWS = 1024
SLOTS = 64
REPLICAS = 8
EXPERTS = 56
CAP = 4
N_EXPERT = 64
N_TENSOR = 8


def plant(array, own_key, smallest, top_value):
    longest = array.shape.index(max(array.shape))
    spots = []
    for shift in (0, 1):
        where = [jax.random.randint(jax.random.fold_in(own_key, axis), (), 0, length) for axis, length in enumerate(array.shape)]
        where[longest] = (where[longest] + shift) % array.shape[longest]
        spots.append(tuple(where))
    return array.at[spots[0]].set(smallest).at[spots[1]].set(top_value)


def block_scale(rng, shape, cuts, least, top_value):
    def one(position, shards_of):
        heights = jax.random.uniform(jax.random.fold_in(jax.random.fold_in(rng, 6), position), (shards_of,), jnp.float32, least / len(cuts), top_value / len(cuts))
        return jnp.repeat(jnp.exp(heights), shape[position] // shards_of).reshape((-1,) + (1,) * (len(shape) - position - 1))

    loudness = one(*cuts[0])
    for cut in cuts[1:]:
        loudness = loudness * one(*cut)
    return loudness


def length_profile(amount, total, bound, skew):
    weights = [(1 << 20) // math.isqrt(rank ** skew) + 1 for rank in range(2, amount + 1)]
    rest, given = total - bound - (amount - 1), [1] * (amount - 1)
    while rest > 0:
        free = [i for i in range(amount - 1) if given[i] < bound]
        whole, left = sum([weights[i] for i in free]), rest
        for i in free:
            addition = min(bound - given[i], max(1, left * weights[i] // whole), rest)
            given[i] = given[i] + addition
            rest = rest - addition
    return np.array([bound] + given)


def uneven(stream_key, number_of, total, most, slope):
    if number_of == 2:
        one = jax.random.randint(stream_key, (), max(1, total - most), min(most, total - 1) + 1)
        return jnp.stack([one, total - one])
    lengths = jnp.asarray(length_profile(number_of, total, most, slope), jnp.int32)
    couples = (number_of - 1) // 2
    donor, taker = lengths[1:1 + 2 * couples:2], lengths[2:2 + 2 * couples:2]
    room = jnp.minimum(donor - 1, most - taker)
    moved = jax.random.randint(jax.random.fold_in(stream_key, 1), (couples,), 0, 1 << 20) % (room + 1)
    lengths = lengths.at[1:1 + 2 * couples:2].set(donor - moved).at[2:2 + 2 * couples:2].set(taker + moved)
    return lengths[jax.random.permutation(jax.random.fold_in(stream_key, 2), number_of)]


def deal_out(key, own, number, rows, amount, top, bound, skew):
    ranking = jax.random.permutation(key, amount)
    crowded, common = load_shares(amount, rows * top, bound, skew, True), load_shares(amount, rows * top, bound, skew, False)
    places = jnp.arange(amount)

    def named(lengths, turn):
        used = int((lengths > 0).sum())
        fixed = max(1, used // 4)
        moved = fixed + (places - fixed + turn * (used - fixed)) % max(1, amount - fixed)
        return jnp.zeros((amount,), jnp.int32).at[ranking[jnp.where(places < fixed, places, moved)]].set(jnp.asarray(lengths, jnp.int32))

    lengths = jnp.where(number % 4 == 0, named(crowded, number // 4), named(common, number - number // 4 - 1))
    mixed = jax.random.permutation(jax.random.fold_in(own, 3), amount)
    donor, receiver = mixed[0:amount // 2 * 2:2], mixed[1:amount // 2 * 2:2]
    margin = jnp.minimum(lengths[donor] - 1, bound - lengths[receiver]) // 2
    margin = jnp.where((donor == ranking[0]) | (receiver == ranking[0]) | (lengths[receiver] == 0), 0, jnp.maximum(margin, 0))
    moved = jax.random.randint(jax.random.fold_in(own, 4), (amount // 2,), 0, 1 << 20) % (margin + 1)
    lengths = lengths.at[donor].add(-moved).at[receiver].add(moved)
    members = jnp.searchsorted(jnp.cumsum(lengths), jnp.arange(rows * top), side="right").astype(jnp.int32)
    table = members.reshape(top, rows).T
    table = table[jax.random.permutation(jax.random.fold_in(own, 1), rows)]
    turn = jax.random.randint(jax.random.fold_in(own, 2), (rows, 1), 0, top)
    return jnp.take_along_axis(table, (jnp.arange(top)[None, :] + turn) % top, axis=1)


def load_shares(count, total, limit, skew, full):
    portions = [(1 << 20) // math.isqrt(grade ** skew) + 1 for grade in range(1, count + 1)]
    largest = limit if full else min(limit, max(-(-total // count), total * portions[0] // sum(portions)))
    least = 1 if total - largest >= count - 1 else 0
    holding, rest = [largest] + [least] * (count - 1), total - largest - least * (count - 1)
    while rest > 0:
        movable = [i for i in range(1, count) if holding[i] < largest] or [i for i in range(1, count) if holding[i] < limit]
        whole, budget = sum([portions[i] for i in movable]), rest
        for i in movable:
            addition = min(limit - holding[i], max(1, budget * portions[i] // whole), rest)
            holding[i] = holding[i] + addition
            rest = rest - addition
    return np.array(holding)


def gaussian(stream_key, shape, deviation, most, split=(), kind=jnp.bfloat16):
    level = block_scale(stream_key, shape, split, -0.22, 0.18) if split else 1.0
    values = jax.random.normal(stream_key, shape, jnp.float32) * deviation * level
    return jnp.minimum(jnp.maximum(values, -most), most).astype(kind)


def setup_inputs(seed: int = 0) -> dict:
    keys = jax.random.split(jax.random.key(seed), 10)
    hidden_rows = gaussian(keys[0], (STEPS, ROWS, D), 1.0, 6.0, ((1, 64), (2, 8)))
    draft_len = jax.vmap(lambda own: uneven(own, REQUESTS, 5 * REQUESTS // 2, SPAN, 2))(jax.random.split(keys[1], STEPS)).reshape((STEPS, REQUESTS)).astype(jnp.int32)
    expert_ids_keys = jax.random.split(jax.random.fold_in(keys[2], 1), STEPS * ROWS // ROWS_DEV)
    expert_ids_turns = jax.random.permutation(jax.random.fold_in(keys[2], 3), STEPS * ROWS // ROWS_DEV)
    expert_ids = jax.vmap(lambda own, number: deal_out(jax.random.fold_in(keys[2], 2), own, number, ROWS_DEV, EXPERTS, TOP, CAP, 2))(expert_ids_keys, expert_ids_turns).reshape((STEPS, ROWS, TOP))
    replica = plant(jax.random.randint(keys[3], (STEPS, ROWS, TOP), 0, 2), jax.random.fold_in(keys[3], 1), 0, 1).astype(jnp.int32)
    route_gain = jnp.clip(jnp.exp(math.log(0.5) - 2.8134107 * jax.random.uniform(keys[4], (STEPS, ROWS, TOP), jnp.float32) ** block_scale(keys[4], (STEPS, ROWS, TOP), ((1, 64),), -0.2, 0.2)), 0.03, 0.5)
    slot_up = gaussian(keys[5], (SLOTS, D, H), D ** -0.5, 0.09375, ((0, 64), (2, 8)))
    slot_down = gaussian(keys[6], (SLOTS, H, D), H ** -0.5, 0.1875, ((0, 64), (1, 8)))
    shared_up = gaussian(keys[7], (D, HS), D ** -0.5, 0.09375, ((1, 8),))
    shared_down = gaussian(keys[8], (HS, D), HS ** -0.5, 0.1875, ((0, 8),))
    return dict(hidden_rows=hidden_rows, draft_len=draft_len, expert_ids=expert_ids, replica=replica, route_gain=route_gain, slot_up=slot_up, slot_down=slot_down, shared_up=shared_up, shared_down=shared_down)


def reference(hidden_rows, draft_len, expert_ids, replica, route_gain, slot_up, slot_down, shared_up, shared_down):
    results = []
    room = N_EXPERT * CAP
    entries_total = ROWS * TOP
    for index in range(STEPS):
        rows_in = hidden_rows[index]
        positions = jnp.arange(ROWS, dtype=jnp.int32)
        live_mask = (positions % SPAN < draft_len[index][positions // SPAN]).astype(jnp.float32)
        chosen = expert_ids[index]
        slot_index = jnp.where((chosen < REPLICAS) & (replica[index] == 1), chosen + EXPERTS, chosen).reshape(-1).astype(jnp.int32)
        valid = jnp.broadcast_to(live_mask[:, None] > 0.5, chosen.shape).reshape(-1)
        onehot = ((slot_index[:, None] == jnp.arange(SLOTS, dtype=jnp.int32)[None, :]) & valid[:, None]).astype(jnp.int32)
        earlier = jnp.cumsum(onehot, axis=0).astype(jnp.int32) - onehot
        order_rank = jnp.sum(earlier * onehot, axis=1).astype(jnp.int32)
        target = jnp.where(valid, slot_index * room + order_rank, SLOTS * room).astype(jnp.int32)
        table = jnp.full((SLOTS * room + 1,), entries_total, jnp.int32)
        table = table.at[target].set(jnp.arange(entries_total, dtype=jnp.int32))
        table = table[:SLOTS * room].reshape(SLOTS, room)
        padded_rows = jnp.concatenate([rows_in, jnp.zeros((1, D), rows_in.dtype)], axis=0)
        flat_gain = jnp.concatenate([(route_gain[index] * live_mask[:, None]).reshape(-1), jnp.zeros((1,), jnp.float32)])

        def serve(total, slot_number):
            entries = table[slot_number]
            row_pick = (entries // TOP).astype(jnp.int32)
            picked = padded_rows[row_pick]
            hidden = jax.nn.silu(jnp.dot(picked, slot_up[slot_number], preferred_element_type=jnp.float32)).astype(jnp.bfloat16)
            parts = jnp.einsum("mth,thd->mtd", hidden.reshape(room, N_TENSOR, H_PART).astype(jnp.float32), slot_down[slot_number].reshape(N_TENSOR, H_PART, D).astype(jnp.float32))
            parts = lax.optimization_barrier(parts.astype(jnp.bfloat16)).astype(jnp.float32)
            combined = jnp.sum(parts, axis=1) * flat_gain[entries][:, None]
            return total.at[row_pick].add(combined), None

        total, _ = lax.scan(serve, jnp.zeros((ROWS + 1, D), jnp.float32), jnp.arange(SLOTS, dtype=jnp.int32))
        shared_act = jax.nn.silu(jnp.dot(rows_in, shared_up, preferred_element_type=jnp.float32)).astype(jnp.bfloat16)
        shared_out = jnp.dot(shared_act, shared_down, preferred_element_type=jnp.float32)
        results.append(((total[:ROWS] + shared_out) * live_mask[:, None]).astype(jnp.bfloat16))
    return jnp.stack(results)
```

```python
import jax
import jax.numpy as jnp
from jax import lax
from jax.sharding import PartitionSpec as P


def route_plan(lengths, chosen, second, gains, slot_count, capacity):
    row_count, top_count = chosen.shape
    span_rows = row_count // lengths.shape[0]
    positions = jnp.arange(row_count, dtype=jnp.int32)
    limit = jnp.repeat(lengths, span_rows, total_repeat_length=row_count)
    live_mask = positions % span_rows < limit
    replicas = slot_count // 8
    experts_all = slot_count - replicas
    slot_index = jnp.where(
        (chosen < replicas) & (second == 1), chosen + experts_all, chosen
    ).reshape(-1)
    valid = jnp.broadcast_to(live_mask[:, None], chosen.shape).reshape(-1)
    onehot = (
        (slot_index[:, None] == jnp.arange(slot_count, dtype=jnp.int32)[None, :]) & valid[:, None]
    ).astype(jnp.int32)
    earlier = jnp.cumsum(onehot, axis=0) - onehot
    order_rank = jnp.sum(earlier * onehot, axis=1)
    target = jnp.where(valid, slot_index * capacity + order_rank, -1)
    buffer_ids = jnp.arange(slot_count * capacity, dtype=jnp.int32)
    picker = jnp.any(
        target.reshape(row_count, top_count)[None, :, :] == buffer_ids[:, None, None], axis=2
    ).astype(jnp.bfloat16)
    weights = (gains * live_mask[:, None].astype(jnp.float32)).reshape(-1)
    return (live_mask, target, picker, weights)


def shards(
    hidden_rows,
    draft_len,
    expert_ids,
    replica,
    route_gain,
    slot_up,
    slot_down,
    shared_up,
    shared_down,
):
    slot_count = lax.axis_size("expert")
    tensor_count = lax.axis_size("tensor")
    step_count, row_count, width_part = hidden_rows.shape
    top_count = expert_ids.shape[2]
    capacity = row_count * top_count // (slot_count - slot_count // 8) + 2
    plans = [
        route_plan(
            draft_len[index],
            expert_ids[index],
            replica[index],
            route_gain[index],
            slot_count,
            capacity,
        )
        for index in range(step_count)
    ]
    outgoing = []
    for index in range(step_count):
        packed = jnp.dot(
            plans[index][2], hidden_rows[index], preferred_element_type=jnp.float32
        ).astype(jnp.bfloat16)
        outgoing.append(packed.reshape(slot_count, capacity, width_part))
    batch = jnp.concatenate(outgoing, axis=1)
    received = lax.all_to_all(batch, "expert", split_axis=0, concat_axis=0, tiled=True)
    served = received.shape[0] * received.shape[1]
    own = step_count * row_count
    rows_part = jnp.concatenate(
        [received.reshape(served, width_part), hidden_rows.reshape(own, width_part)], axis=0
    )
    rows_all = lax.all_gather(rows_part, "tensor", axis=0, tiled=False)
    up_w = slot_up[0].reshape(tensor_count, width_part, -1)
    shared_w = shared_up.reshape(tensor_count, width_part, -1)
    hidden = jax.nn.silu(
        jnp.einsum("tmc,tch->mh", rows_all[:, :served], up_w, preferred_element_type=jnp.float32)
    ).astype(jnp.bfloat16)
    shared_act = jax.nn.silu(
        jnp.einsum("tmc,tch->mh", rows_all[:, served:], shared_w, preferred_element_type=jnp.float32)
    ).astype(jnp.bfloat16)
    down_w = slot_down[0].reshape(-1, tensor_count, width_part)
    shared_dw = shared_down.reshape(-1, tensor_count, width_part)
    part_value = jnp.einsum(
        "mh,htc->tmc", hidden, down_w, preferred_element_type=jnp.float32
    ).astype(jnp.bfloat16)
    shared_value = jnp.einsum(
        "mh,htc->tmc", shared_act, shared_dw, preferred_element_type=jnp.float32
    ).astype(jnp.bfloat16)
    both = jnp.concatenate([part_value, shared_value], axis=1)
    summed = lax.psum_scatter(both, "tensor", scatter_dimension=0, tiled=True)[0]
    routed_back = summed[:served].reshape(received.shape)
    shared_own = summed[served:].astype(jnp.float32).reshape(step_count, row_count, width_part)
    answer = lax.all_to_all(routed_back, "expert", split_axis=0, concat_axis=0, tiled=True)
    results = []
    for index in range(step_count):
        live_mask, target, picker, weights = plans[index]
        slot_rows = answer[:, index * capacity : (index + 1) * capacity].reshape(-1, width_part)
        fetched = jnp.take(slot_rows, jnp.maximum(target, 0), axis=0).astype(jnp.float32)
        routed = jnp.sum(
            (fetched * weights[:, None]).reshape(row_count, top_count, width_part), axis=1
        )
        live = live_mask.astype(jnp.float32)[:, None]
        results.append(((routed + shared_own[index]) * live).astype(jnp.bfloat16))
    return jnp.stack(results)


def solution(mesh):
    return jax.shard_map(
        shards,
        mesh=mesh,
        in_specs=(
            P(None, "expert", "tensor"),
            P(None, "expert"),
            P(None, "expert", None),
            P(None, "expert", None),
            P(None, "expert", None),
            P("expert", None, "tensor"),
            P("expert", "tensor", None),
            P(None, "tensor"),
            P("tensor", None),
        ),
        out_specs=P(None, "expert", "tensor"),
        check_vma=False,
    )
```

```python
import jax
import jax.numpy as jnp
from jax import lax
from jax.sharding import PartitionSpec as P


def route_plan(lengths, chosen, second, gains, slot_count, capacity):
    row_count, top_count = chosen.shape
    span_rows = row_count // lengths.shape[0]
    positions = jnp.arange(row_count, dtype=jnp.int32)
    limit = jnp.repeat(lengths, span_rows, total_repeat_length=row_count)
    live_mask = positions % span_rows < limit
    replicas = slot_count // 8
    experts_all = slot_count - replicas
    slot_index = jnp.where(
        (chosen < replicas) & (second == 1), chosen + experts_all, chosen
    ).reshape(-1)
    valid = jnp.broadcast_to(live_mask[:, None], chosen.shape).reshape(-1)
    onehot = (
        (slot_index[:, None] == jnp.arange(slot_count, dtype=jnp.int32)[None, :]) & valid[:, None]
    ).astype(jnp.int32)
    earlier = jnp.cumsum(onehot, axis=0) - onehot
    order_rank = jnp.sum(earlier * onehot, axis=1)
    target = jnp.where(valid, slot_index * capacity + order_rank, -1)
    buffer_ids = jnp.arange(slot_count * capacity, dtype=jnp.int32)
    picker = jnp.any(
        target.reshape(row_count, top_count)[None, :, :] == buffer_ids[:, None, None], axis=2
    ).astype(jnp.bfloat16)
    weights = (gains * live_mask[:, None].astype(jnp.float32)).reshape(-1)
    return (live_mask, target, picker, weights)


def shards(
    hidden_rows,
    draft_len,
    expert_ids,
    replica,
    route_gain,
    slot_up,
    slot_down,
    shared_up,
    shared_down,
):
    slot_count = lax.axis_size("expert")
    tensor_count = lax.axis_size("tensor")
    step_count, row_count, width_part = hidden_rows.shape
    top_count = expert_ids.shape[2]
    capacity = row_count * top_count // (slot_count - slot_count // 8) + 2
    plans = [
        route_plan(
            draft_len[index],
            expert_ids[index],
            replica[index],
            route_gain[index],
            slot_count,
            capacity,
        )
        for index in range(step_count)
    ]
    outgoing = []
    for index in range(step_count):
        packed = jnp.dot(
            plans[index][2], hidden_rows[index], preferred_element_type=jnp.float32
        ).astype(jnp.bfloat16)
        outgoing.append(packed.reshape(slot_count, capacity, width_part))
    batch = jnp.concatenate(outgoing, axis=1)
    received = lax.all_to_all(batch, "expert", split_axis=0, concat_axis=0, tiled=True)
    served = received.shape[0] * received.shape[1]
    own = step_count * row_count
    rows_part = jnp.concatenate(
        [received.reshape(served, width_part), hidden_rows.reshape(own, width_part)], axis=0
    )
    rows_all = lax.all_gather(rows_part, "tensor", axis=0, tiled=False)
    hidden_units = slot_up.shape[2]
    up_w = jnp.concatenate([slot_up[0], shared_up], axis=1).reshape(tensor_count, width_part, -1)
    up_value = jnp.einsum("tmc,tch->mh", rows_all, up_w, preferred_element_type=jnp.float32)
    act = jax.nn.silu(up_value).astype(jnp.bfloat16)
    is_routed = (jnp.arange(served + own) < served)[:, None]
    act_ext = jnp.concatenate(
        [
            jnp.where(is_routed, act[:, :hidden_units], jnp.zeros_like(act[:, :hidden_units])),
            jnp.where(is_routed, jnp.zeros_like(act[:, hidden_units:]), act[:, hidden_units:]),
        ],
        axis=1,
    )
    down_w = jnp.concatenate([slot_down[0], shared_down], axis=0)
    down_w = down_w.reshape(-1, tensor_count, width_part).transpose(1, 0, 2)
    act_b = jnp.broadcast_to(act_ext[None], (tensor_count,) + act_ext.shape)
    both = jnp.einsum(
        "tmh,thc->tmc", act_b, down_w, preferred_element_type=jnp.float32
    ).astype(jnp.bfloat16)
    summed = lax.psum_scatter(both, "tensor", scatter_dimension=0, tiled=True)[0]
    routed_back = summed[:served].reshape(received.shape)
    shared_own = summed[served:].astype(jnp.float32).reshape(step_count, row_count, width_part)
    answer = lax.all_to_all(routed_back, "expert", split_axis=0, concat_axis=0, tiled=True)
    results = []
    for index in range(step_count):
        live_mask, target, picker, weights = plans[index]
        slot_rows = answer[:, index * capacity : (index + 1) * capacity].reshape(-1, width_part)
        fetched = jnp.take(slot_rows, jnp.maximum(target, 0), axis=0).astype(jnp.float32)
        routed = jnp.sum(
            (fetched * weights[:, None]).reshape(row_count, top_count, width_part), axis=1
        )
        live = live_mask.astype(jnp.float32)[:, None]
        results.append(((routed + shared_own[index]) * live).astype(jnp.bfloat16))
    return jnp.stack(results)


def solution(mesh):
    return jax.shard_map(
        shards,
        mesh=mesh,
        in_specs=(
            P(None, "expert", "tensor"),
            P(None, "expert"),
            P(None, "expert", None),
            P(None, "expert", None),
            P(None, "expert", None),
            P("expert", None, "tensor"),
            P("expert", "tensor", None),
            P(None, "tensor"),
            P("tensor", None),
        ),
        out_specs=P(None, "expert", "tensor"),
        check_vma=False,
    )
```

```python
import jax
import jax.numpy as jnp
from jax import lax
from jax.sharding import PartitionSpec as P


def route_plan(lengths, chosen, second, gains, slot_count, capacity):
    row_count, top_count = chosen.shape
    span_rows = row_count // lengths.shape[0]
    positions = jnp.arange(row_count, dtype=jnp.int32)
    limit = jnp.repeat(lengths, span_rows, total_repeat_length=row_count)
    live_mask = positions % span_rows < limit
    replicas = slot_count // 8
    experts_all = slot_count - replicas
    slot_index = jnp.where(
        (chosen < replicas) & (second == 1), chosen + experts_all, chosen
    ).reshape(-1)
    valid = jnp.broadcast_to(live_mask[:, None], chosen.shape).reshape(-1)
    onehot = (
        (slot_index[:, None] == jnp.arange(slot_count, dtype=jnp.int32)[None, :]) & valid[:, None]
    ).astype(jnp.int32)
    earlier = jnp.cumsum(onehot, axis=0) - onehot
    order_rank = jnp.sum(earlier * onehot, axis=1)
    target = jnp.where(valid, slot_index * capacity + order_rank, -1)
    buffer_ids = jnp.arange(slot_count * capacity, dtype=jnp.int32)
    picker = jnp.any(
        target.reshape(row_count, top_count)[None, :, :] == buffer_ids[:, None, None], axis=2
    ).astype(jnp.bfloat16)
    weights = (gains * live_mask[:, None].astype(jnp.float32)).reshape(-1)
    return (live_mask, target, picker, weights)


def shards(
    hidden_rows,
    draft_len,
    expert_ids,
    replica,
    route_gain,
    slot_up,
    slot_down,
    shared_up,
    shared_down,
):
    slot_count = lax.axis_size("expert")
    tensor_count = lax.axis_size("tensor")
    step_count, row_count, width_part = hidden_rows.shape
    top_count = expert_ids.shape[2]
    capacity = row_count * top_count // (slot_count - slot_count // 8) + 2
    plans = [
        route_plan(
            draft_len[index],
            expert_ids[index],
            replica[index],
            route_gain[index],
            slot_count,
            capacity,
        )
        for index in range(step_count)
    ]
    hidden_units = slot_up.shape[2]
    down_parts = jnp.concatenate([slot_down[0], shared_down], axis=0)
    down_parts = down_parts.reshape(-1, tensor_count, width_part).transpose(1, 0, 2)
    down_cols = lax.all_to_all(down_parts, "tensor", split_axis=0, concat_axis=0, tiled=True)
    outgoing = []
    for index in range(step_count):
        packed = jnp.dot(
            plans[index][2], hidden_rows[index], preferred_element_type=jnp.float32
        ).astype(jnp.bfloat16)
        outgoing.append(packed.reshape(slot_count, capacity, width_part))
    batch = jnp.concatenate(outgoing, axis=1)
    received = lax.all_to_all(batch, "expert", split_axis=0, concat_axis=0, tiled=True)
    served = received.shape[0] * received.shape[1]
    own = step_count * row_count
    rows_part = jnp.concatenate(
        [received.reshape(served, width_part), hidden_rows.reshape(own, width_part)], axis=0
    )
    rows_all = lax.all_gather(rows_part, "tensor", axis=0, tiled=False)
    up_w = jnp.concatenate([slot_up[0], shared_up], axis=1).reshape(tensor_count, width_part, -1)
    up_value = jnp.einsum("tmc,tch->mh", rows_all, up_w, preferred_element_type=jnp.float32)
    act = jax.nn.silu(up_value).astype(jnp.bfloat16)
    is_routed = (jnp.arange(served + own) < served)[:, None]
    act_own = jnp.where(is_routed, act[:, :hidden_units], act[:, hidden_units:])
    act_all = lax.all_gather(act_own, "tensor", axis=0, tiled=False)
    routed_back = jnp.einsum(
        "imu,iuc->mc",
        act_all[:, :served],
        down_cols[:, :hidden_units],
        preferred_element_type=jnp.float32,
    ).astype(jnp.bfloat16).reshape(received.shape)
    shared_own = jnp.einsum(
        "imu,iuc->mc",
        act_all[:, served:],
        down_cols[:, hidden_units:],
        preferred_element_type=jnp.float32,
    ).reshape(step_count, row_count, width_part)
    answer = lax.all_to_all(routed_back, "expert", split_axis=0, concat_axis=0, tiled=True)
    results = []
    for index in range(step_count):
        live_mask, target, picker, weights = plans[index]
        slot_rows = answer[:, index * capacity : (index + 1) * capacity].reshape(-1, width_part)
        fetched = jnp.take(slot_rows, jnp.maximum(target, 0), axis=0).astype(jnp.float32)
        routed = jnp.sum(
            (fetched * weights[:, None]).reshape(row_count, top_count, width_part), axis=1
        )
        live = live_mask.astype(jnp.float32)[:, None]
        results.append(((routed + shared_own[index]) * live).astype(jnp.bfloat16))
    return jnp.stack(results)


def solution(mesh):
    return jax.shard_map(
        shards,
        mesh=mesh,
        in_specs=(
            P(None, "expert", "tensor"),
            P(None, "expert"),
            P(None, "expert", None),
            P(None, "expert", None),
            P(None, "expert", None),
            P("expert", None, "tensor"),
            P("expert", "tensor", None),
            P(None, "tensor"),
            P("tensor", None),
        ),
        out_specs=P(None, "expert", "tensor"),
        check_vma=False,
    )
```

```python
import jax
import jax.numpy as jnp
from jax import lax
from jax.sharding import PartitionSpec as P


def route_plan(lengths, chosen, second, gains, slot_count, capacity):
    row_count, top_count = chosen.shape
    span_rows = row_count // lengths.shape[0]
    positions = jnp.arange(row_count, dtype=jnp.int32)
    limit = jnp.repeat(lengths, span_rows, total_repeat_length=row_count)
    live_mask = positions % span_rows < limit
    replicas = slot_count // 8
    experts_all = slot_count - replicas
    slot_index = jnp.where(
        (chosen < replicas) & (second == 1), chosen + experts_all, chosen
    ).reshape(-1)
    valid = jnp.broadcast_to(live_mask[:, None], chosen.shape).reshape(-1)
    onehot = (
        (slot_index[:, None] == jnp.arange(slot_count, dtype=jnp.int32)[None, :]) & valid[:, None]
    ).astype(jnp.int32)
    earlier = jnp.cumsum(onehot, axis=0) - onehot
    order_rank = jnp.sum(earlier * onehot, axis=1)
    target = jnp.where(valid, slot_index * capacity + order_rank, -1)
    buffer_ids = jnp.arange(slot_count * capacity, dtype=jnp.int32)
    picker = jnp.any(
        target.reshape(row_count, top_count)[None, :, :] == buffer_ids[:, None, None], axis=2
    ).astype(jnp.bfloat16)
    weights = (gains * live_mask[:, None].astype(jnp.float32)).reshape(-1)
    return (live_mask, target, picker, weights)


def shards(
    hidden_rows,
    draft_len,
    expert_ids,
    replica,
    route_gain,
    slot_up,
    slot_down,
    shared_up,
    shared_down,
):
    slot_count = lax.axis_size("expert")
    tensor_count = lax.axis_size("tensor")
    step_count, row_count, width_part = hidden_rows.shape
    top_count = expert_ids.shape[2]
    capacity = row_count * top_count // (slot_count - slot_count // 8) + 2
    plans = [
        route_plan(
            draft_len[index],
            expert_ids[index],
            replica[index],
            route_gain[index],
            slot_count,
            capacity,
        )
        for index in range(step_count)
    ]
    hidden_units = slot_up.shape[2]
    down_parts = jnp.concatenate([slot_down[0], shared_down], axis=0)
    down_parts = down_parts.reshape(-1, tensor_count, width_part).transpose(1, 0, 2)
    me = lax.axis_index("tensor")
    received_parts = [lax.dynamic_index_in_dim(down_parts, me, 0, keepdims=False)]
    for shift in range(1, tensor_count):
        piece = lax.dynamic_index_in_dim(down_parts, (me + shift) % tensor_count, 0, keepdims=False)
        pairs = [(i, (i + shift) % tensor_count) for i in range(tensor_count)]
        received_parts.append(lax.ppermute(piece, "tensor", pairs))
    down_cols = jnp.stack(received_parts)
    source_order = (me - jnp.arange(tensor_count, dtype=jnp.int32)) % tensor_count
    outgoing = []
    for index in range(step_count):
        packed = jnp.dot(
            plans[index][2], hidden_rows[index], preferred_element_type=jnp.float32
        ).astype(jnp.bfloat16)
        outgoing.append(packed.reshape(slot_count, capacity, width_part))
    batch = jnp.concatenate(outgoing, axis=1)
    received = lax.all_to_all(batch, "expert", split_axis=0, concat_axis=0, tiled=True)
    served = received.shape[0] * received.shape[1]
    own = step_count * row_count
    rows_part = jnp.concatenate(
        [received.reshape(served, width_part), hidden_rows.reshape(own, width_part)], axis=0
    )
    rows_all = lax.all_gather(rows_part, "tensor", axis=0, tiled=False)
    up_w = jnp.concatenate([slot_up[0], shared_up], axis=1).reshape(tensor_count, width_part, -1)
    up_value = jnp.einsum("tmc,tch->mh", rows_all, up_w, preferred_element_type=jnp.float32)
    act = jax.nn.silu(up_value).astype(jnp.bfloat16)
    is_routed = (jnp.arange(served + own) < served)[:, None]
    act_own = jnp.where(is_routed, act[:, :hidden_units], act[:, hidden_units:])
    act_all = jnp.take(lax.all_gather(act_own, "tensor", axis=0, tiled=False), source_order, axis=0)
    routed_back = jnp.einsum(
        "imu,iuc->mc",
        act_all[:, :served],
        down_cols[:, :hidden_units],
        preferred_element_type=jnp.float32,
    ).astype(jnp.bfloat16).reshape(received.shape)
    shared_own = jnp.einsum(
        "imu,iuc->mc",
        act_all[:, served:],
        down_cols[:, hidden_units:],
        preferred_element_type=jnp.float32,
    ).reshape(step_count, row_count, width_part)
    answer = lax.all_to_all(routed_back, "expert", split_axis=0, concat_axis=0, tiled=True)
    results = []
    for index in range(step_count):
        live_mask, target, picker, weights = plans[index]
        slot_rows = answer[:, index * capacity : (index + 1) * capacity].reshape(-1, width_part)
        fetched = jnp.take(slot_rows, jnp.maximum(target, 0), axis=0).astype(jnp.float32)
        routed = jnp.sum(
            (fetched * weights[:, None]).reshape(row_count, top_count, width_part), axis=1
        )
        live = live_mask.astype(jnp.float32)[:, None]
        results.append(((routed + shared_own[index]) * live).astype(jnp.bfloat16))
    return jnp.stack(results)


def solution(mesh):
    return jax.shard_map(
        shards,
        mesh=mesh,
        in_specs=(
            P(None, "expert", "tensor"),
            P(None, "expert"),
            P(None, "expert", None),
            P(None, "expert", None),
            P(None, "expert", None),
            P("expert", None, "tensor"),
            P("expert", "tensor", None),
            P(None, "tensor"),
            P("tensor", None),
        ),
        out_specs=P(None, "expert", "tensor"),
        check_vma=False,
    )
```

```python
import jax
import jax.numpy as jnp
from jax import lax
from jax.sharding import PartitionSpec as P


def route_plan(lengths, chosen, second, gains, slot_count, capacity):
    row_count, top_count = chosen.shape
    span_rows = row_count // lengths.shape[0]
    positions = jnp.arange(row_count, dtype=jnp.int32)
    limit = jnp.repeat(lengths, span_rows, total_repeat_length=row_count)
    live_mask = positions % span_rows < limit
    replicas = slot_count // 8
    experts_all = slot_count - replicas
    slot_index = jnp.where(
        (chosen < replicas) & (second == 1), chosen + experts_all, chosen
    ).reshape(-1)
    valid = jnp.broadcast_to(live_mask[:, None], chosen.shape).reshape(-1)
    onehot = (
        (slot_index[:, None] == jnp.arange(slot_count, dtype=jnp.int32)[None, :]) & valid[:, None]
    ).astype(jnp.int32)
    earlier = jnp.cumsum(onehot, axis=0) - onehot
    order_rank = jnp.sum(earlier * onehot, axis=1)
    target = jnp.where(valid, slot_index * capacity + order_rank, -1)
    buffer_ids = jnp.arange(slot_count * capacity, dtype=jnp.int32)
    picker = jnp.any(
        target.reshape(row_count, top_count)[None, :, :] == buffer_ids[:, None, None], axis=2
    ).astype(jnp.bfloat16)
    weights = (gains * live_mask[:, None].astype(jnp.float32)).reshape(-1)
    return (live_mask, target, picker, weights)


def layer(
    hidden_rows,
    draft_len,
    expert_ids,
    replica,
    route_gain,
    slot_up,
    slot_down,
    shared_up,
    shared_down,
):
    slot_count = lax.axis_size("expert")
    tensor_count = lax.axis_size("tensor")
    step_count, row_count, width_part = hidden_rows.shape
    top_count = expert_ids.shape[2]
    capacity = row_count * top_count // (slot_count - slot_count // 8) + 2
    plans = [
        route_plan(
            draft_len[index],
            expert_ids[index],
            replica[index],
            route_gain[index],
            slot_count,
            capacity,
        )
        for index in range(step_count)
    ]
    hidden_units = slot_up.shape[2]
    down_parts = jnp.concatenate([slot_down[0], shared_down], axis=0)
    down_parts = down_parts.reshape(-1, tensor_count, width_part).transpose(1, 0, 2)
    down_cols = lax.all_to_all(down_parts, "tensor", split_axis=0, concat_axis=0, tiled=True)
    outgoing = []
    for index in range(step_count):
        packed = jnp.dot(
            plans[index][2], hidden_rows[index], preferred_element_type=jnp.float32
        ).astype(jnp.bfloat16)
        outgoing.append(packed.reshape(slot_count, capacity, width_part))
    batch = jnp.concatenate(outgoing, axis=1)
    received = lax.all_to_all(batch, "expert", split_axis=0, concat_axis=0, tiled=True)
    served = received.shape[0] * received.shape[1]
    own = step_count * row_count
    rows_part = jnp.concatenate(
        [received.reshape(served, width_part), hidden_rows.reshape(own, width_part)], axis=0
    )
    rows_all = lax.all_gather(rows_part, "tensor", axis=0, tiled=False)
    up_w = jnp.concatenate([slot_up[0], shared_up], axis=1).reshape(tensor_count, width_part, -1)
    up_value = jnp.einsum("tmc,tch->mh", rows_all, up_w, preferred_element_type=jnp.float32)
    act = jax.nn.silu(up_value).astype(jnp.bfloat16)
    is_routed = (jnp.arange(served + own) < served)[:, None]
    act_own = jnp.where(is_routed, act[:, :hidden_units], act[:, hidden_units:])
    act_all = lax.all_gather(act_own, "tensor", axis=0, tiled=False)
    routed_back = jnp.einsum(
        "imu,iuc->mc",
        act_all[:, :served],
        down_cols[:, :hidden_units],
        preferred_element_type=jnp.float32,
    ).astype(jnp.bfloat16).reshape(received.shape)
    shared_own = jnp.einsum(
        "imu,iuc->mc",
        act_all[:, served:],
        down_cols[:, hidden_units:],
        preferred_element_type=jnp.float32,
    ).reshape(step_count, row_count, width_part)
    answer = lax.all_to_all(routed_back, "expert", split_axis=0, concat_axis=0, tiled=True)
    results = []
    for index in range(step_count):
        live_mask, target, _, weights = plans[index]
        slot_rows = answer[:, index * capacity : (index + 1) * capacity].reshape(-1, width_part)
        fetched = jnp.take(slot_rows, jnp.maximum(target, 0), axis=0).astype(jnp.float32)
        routed = jnp.sum(
            (fetched * weights[:, None]).reshape(row_count, top_count, width_part), axis=1
        )
        live = live_mask.astype(jnp.float32)[:, None]
        results.append(((routed + shared_own[index]) * live).astype(jnp.bfloat16))
    return jnp.stack(results)


def solution(mesh):
    return jax.shard_map(
        layer,
        mesh=mesh,
        in_specs=(
            P(None, "expert", "tensor"),
            P(None, "expert"),
            P(None, "expert", None),
            P(None, "expert", None),
            P(None, "expert", None),
            P("expert", None, "tensor"),
            P("expert", "tensor", None),
            P(None, "tensor"),
            P("tensor", None),
        ),
        out_specs=P(None, "expert", "tensor"),
        check_vma=False,
    )
```

```python
import jax
import jax.numpy as jnp
from jax import lax
from jax.sharding import PartitionSpec as P


def route_plan(lengths, chosen, second, gains, slot_count, capacity):
    row_count, top_count = chosen.shape
    span_rows = row_count // lengths.shape[0]
    positions = jnp.arange(row_count, dtype=jnp.int32)
    limit = jnp.repeat(lengths, span_rows, total_repeat_length=row_count)
    live_mask = positions % span_rows < limit
    replicas = slot_count // 8
    experts_all = slot_count - replicas
    slot_index = jnp.where(
        (chosen < replicas) & (second == 1), chosen + experts_all, chosen
    ).reshape(-1)
    valid = jnp.broadcast_to(live_mask[:, None], chosen.shape).reshape(-1)
    onehot = (
        (slot_index[:, None] == jnp.arange(slot_count, dtype=jnp.int32)[None, :]) & valid[:, None]
    ).astype(jnp.int32)
    earlier = jnp.cumsum(onehot, axis=0) - onehot
    order_rank = jnp.sum(earlier * onehot, axis=1)
    target = jnp.where(valid, slot_index * capacity + order_rank, -1)
    buffer_ids = jnp.arange(slot_count * capacity, dtype=jnp.int32)
    picker = jnp.any(
        target.reshape(row_count, top_count)[None, :, :] == buffer_ids[:, None, None], axis=2
    ).astype(jnp.bfloat16)
    weights = (gains * live_mask[:, None].astype(jnp.float32)).reshape(-1)
    return (live_mask, target, picker, weights)


def layer(
    hidden_rows,
    draft_len,
    expert_ids,
    replica,
    route_gain,
    slot_up,
    slot_down,
    shared_up,
    shared_down,
):
    slot_count = lax.axis_size("expert")
    tensor_count = lax.axis_size("tensor")
    step_count, row_count, width_part = hidden_rows.shape
    top_count = expert_ids.shape[2]
    capacity = row_count * top_count // (slot_count - slot_count // 8) + 2
    plans = [
        route_plan(
            draft_len[index],
            expert_ids[index],
            replica[index],
            route_gain[index],
            slot_count,
            capacity,
        )
        for index in range(step_count)
    ]
    hidden_units = slot_up.shape[2]
    down_parts = jnp.concatenate([slot_down[0], shared_down], axis=0)
    down_parts = down_parts.reshape(-1, tensor_count, width_part).transpose(1, 0, 2)
    me = lax.axis_index("tensor")
    received_parts = [lax.dynamic_index_in_dim(down_parts, me, 0, keepdims=False)]
    for shift in range(1, tensor_count):
        piece = lax.dynamic_index_in_dim(down_parts, (me + shift) % tensor_count, 0, keepdims=False)
        pairs = [(i, (i + shift) % tensor_count) for i in range(tensor_count)]
        received_parts.append(lax.ppermute(piece, "tensor", pairs))
    outgoing = []
    for index in range(step_count):
        packed = jnp.dot(
            plans[index][2], hidden_rows[index], preferred_element_type=jnp.float32
        ).astype(jnp.bfloat16)
        outgoing.append(packed.reshape(slot_count, capacity, width_part))
    batch = jnp.concatenate(outgoing, axis=1)
    received = lax.all_to_all(batch, "expert", split_axis=0, concat_axis=0, tiled=True)
    served = received.shape[0] * received.shape[1]
    own = step_count * row_count
    rows_part = jnp.concatenate(
        [received.reshape(served, width_part), hidden_rows.reshape(own, width_part)], axis=0
    )
    rows_all = lax.all_gather(rows_part, "tensor", axis=0, tiled=False)
    up_w = jnp.concatenate([slot_up[0], shared_up], axis=1).reshape(tensor_count, width_part, -1)
    up_value = jnp.einsum("tmc,tch->mh", rows_all, up_w, preferred_element_type=jnp.float32)
    act = jax.nn.silu(up_value).astype(jnp.bfloat16)
    is_routed = (jnp.arange(served + own) < served)[:, None]
    act_own = jnp.where(is_routed, act[:, :hidden_units], act[:, hidden_units:])
    act_all = lax.all_gather(act_own, "tensor", axis=0, tiled=False)
    routed_sum = None
    shared_sum = None
    for shift, part in enumerate(received_parts):
        act_part = lax.dynamic_index_in_dim(act_all, (me - shift) % tensor_count, 0, keepdims=False)
        routed_term = jnp.dot(
            act_part[:served], part[:hidden_units], preferred_element_type=jnp.float32
        )
        shared_term = jnp.dot(
            act_part[served:], part[hidden_units:], preferred_element_type=jnp.float32
        )
        routed_sum = routed_term if routed_sum is None else routed_sum + routed_term
        shared_sum = shared_term if shared_sum is None else shared_sum + shared_term
    routed_back = routed_sum.astype(jnp.bfloat16).reshape(received.shape)
    shared_own = shared_sum.reshape(step_count, row_count, width_part)
    answer = lax.all_to_all(routed_back, "expert", split_axis=0, concat_axis=0, tiled=True)
    results = []
    for index in range(step_count):
        live_mask, target, _, weights = plans[index]
        slot_rows = answer[:, index * capacity : (index + 1) * capacity].reshape(-1, width_part)
        fetched = jnp.take(slot_rows, jnp.maximum(target, 0), axis=0).astype(jnp.float32)
        routed = jnp.sum(
            (fetched * weights[:, None]).reshape(row_count, top_count, width_part), axis=1
        )
        live = live_mask.astype(jnp.float32)[:, None]
        results.append(((routed + shared_own[index]) * live).astype(jnp.bfloat16))
    return jnp.stack(results)


def solution(mesh):
    return jax.shard_map(
        layer,
        mesh=mesh,
        in_specs=(
            P(None, "expert", "tensor"),
            P(None, "expert"),
            P(None, "expert", None),
            P(None, "expert", None),
            P(None, "expert", None),
            P("expert", None, "tensor"),
            P("expert", "tensor", None),
            P(None, "tensor"),
            P("tensor", None),
        ),
        out_specs=P(None, "expert", "tensor"),
        check_vma=False,
    )
```

```python
import jax
import jax.numpy as jnp
from jax import lax
from jax.sharding import PartitionSpec as P


def route_plan(lengths, chosen, second, gains, slot_count, capacity):
    step_count, row_count, top_count = chosen.shape
    span_rows = row_count // lengths.shape[1]
    positions = jnp.arange(row_count, dtype=jnp.int32)
    limit = jnp.repeat(lengths, span_rows, axis=1, total_repeat_length=row_count)
    live_mask = positions[None, :] % span_rows < limit
    replicas = slot_count // 8
    experts_all = slot_count - replicas
    slot_index = jnp.where(
        (chosen < replicas) & (second == 1), chosen + experts_all, chosen
    ).reshape(step_count, -1)
    valid = jnp.broadcast_to(live_mask[:, :, None], chosen.shape).reshape(step_count, -1)
    onehot = (
        (slot_index[:, :, None] == jnp.arange(slot_count, dtype=jnp.int32)[None, None, :])
        & valid[:, :, None]
    ).astype(jnp.int32)
    earlier = jnp.cumsum(onehot, axis=1) - onehot
    order_rank = jnp.sum(earlier * onehot, axis=2)
    step_ids = jnp.arange(step_count, dtype=jnp.int32)[:, None]
    place = (slot_index * step_count + step_ids) * capacity + order_rank
    target = jnp.where(valid, place, -1).reshape(step_count, row_count, top_count)
    buffer_ids = jnp.arange(slot_count * step_count * capacity, dtype=jnp.int32)
    picker = jnp.any(
        target.reshape(step_count * row_count, top_count)[None, :, :]
        == buffer_ids[:, None, None],
        axis=2,
    ).astype(jnp.bfloat16)
    weights = gains * live_mask[:, :, None].astype(jnp.float32)
    return (live_mask, target, picker, weights)


def shards(
    hidden_rows,
    draft_len,
    expert_ids,
    replica,
    route_gain,
    slot_up,
    slot_down,
    shared_up,
    shared_down,
):
    slot_count = lax.axis_size("expert")
    tensor_count = lax.axis_size("tensor")
    step_count, row_count, width_part = hidden_rows.shape
    top_count = expert_ids.shape[2]
    capacity = row_count * top_count // (slot_count - slot_count // 8) + 2
    live_mask, target, picker, weights = route_plan(
        draft_len, expert_ids, replica, route_gain, slot_count, capacity
    )
    hidden_units = slot_up.shape[2]
    down_parts = jnp.concatenate([slot_down[0], shared_down], axis=0)
    down_parts = down_parts.reshape(-1, tensor_count, width_part).transpose(1, 0, 2)
    down_cols = lax.all_to_all(down_parts, "tensor", split_axis=0, concat_axis=0, tiled=True)
    batch = jnp.dot(
        picker,
        hidden_rows.reshape(step_count * row_count, width_part),
        preferred_element_type=jnp.float32,
    ).astype(jnp.bfloat16).reshape(slot_count, step_count * capacity, width_part)
    received = lax.all_to_all(batch, "expert", split_axis=0, concat_axis=0, tiled=True)
    served = received.shape[0] * received.shape[1]
    own = step_count * row_count
    rows_part = jnp.concatenate(
        [received.reshape(served, width_part), hidden_rows.reshape(own, width_part)], axis=0
    )
    rows_all = lax.all_gather(rows_part, "tensor", axis=0, tiled=False)
    up_w = jnp.concatenate([slot_up[0], shared_up], axis=1).reshape(tensor_count, width_part, -1)
    up_value = jnp.einsum("tmc,tch->mh", rows_all, up_w, preferred_element_type=jnp.float32)
    act = jax.nn.silu(up_value).astype(jnp.bfloat16)
    is_routed = (jnp.arange(served + own) < served)[:, None]
    act_own = jnp.where(is_routed, act[:, :hidden_units], act[:, hidden_units:])
    act_all = lax.all_gather(act_own, "tensor", axis=0, tiled=False)
    routed_back = jnp.einsum(
        "imu,iuc->mc",
        act_all[:, :served],
        down_cols[:, :hidden_units],
        preferred_element_type=jnp.float32,
    ).astype(jnp.bfloat16).reshape(received.shape)
    shared_own = jnp.einsum(
        "imu,iuc->mc",
        act_all[:, served:],
        down_cols[:, hidden_units:],
        preferred_element_type=jnp.float32,
    ).reshape(step_count, row_count, width_part)
    answer = lax.all_to_all(routed_back, "expert", split_axis=0, concat_axis=0, tiled=True)
    slot_rows = answer.reshape(-1, width_part)
    fetched = jnp.take(slot_rows, jnp.maximum(target, 0).reshape(-1), axis=0).astype(jnp.float32)
    fetched = fetched.reshape(step_count, row_count, top_count, width_part)
    routed = jnp.sum(fetched * weights[:, :, :, None], axis=2)
    live = live_mask.astype(jnp.float32)[:, :, None]
    return ((routed + shared_own) * live).astype(jnp.bfloat16)


def solution(mesh):
    return jax.shard_map(
        shards,
        mesh=mesh,
        in_specs=(
            P(None, "expert", "tensor"),
            P(None, "expert"),
            P(None, "expert", None),
            P(None, "expert", None),
            P(None, "expert", None),
            P("expert", None, "tensor"),
            P("expert", "tensor", None),
            P(None, "tensor"),
            P("tensor", None),
        ),
        out_specs=P(None, "expert", "tensor"),
        check_vma=False,
    )
```

```python
import jax
import jax.numpy as jnp
from jax import lax
from jax.sharding import Mesh, PartitionSpec as P

TENSOR = ("tx", "tc")


def route_plan(lengths, chosen, second, gains, slot_count, capacity):
    step_count, row_count, top_count = chosen.shape
    span_rows = row_count // lengths.shape[1]
    positions = jnp.arange(row_count, dtype=jnp.int32)
    limit = jnp.repeat(lengths, span_rows, axis=1, total_repeat_length=row_count)
    live_mask = positions[None, :] % span_rows < limit
    replicas = slot_count // 8
    experts_all = slot_count - replicas
    slot_index = jnp.where(
        (chosen < replicas) & (second == 1), chosen + experts_all, chosen
    ).reshape(step_count, -1)
    valid = jnp.broadcast_to(live_mask[:, :, None], chosen.shape).reshape(step_count, -1)
    onehot = (
        (slot_index[:, :, None] == jnp.arange(slot_count, dtype=jnp.int32)[None, None, :])
        & valid[:, :, None]
    ).astype(jnp.int32)
    earlier = jnp.cumsum(onehot, axis=1) - onehot
    order_rank = jnp.sum(earlier * onehot, axis=2)
    step_ids = jnp.arange(step_count, dtype=jnp.int32)[:, None]
    place = (slot_index * step_count + step_ids) * capacity + order_rank
    target = jnp.where(valid, place, -1).reshape(step_count, row_count, top_count)
    buffer_ids = jnp.arange(slot_count * step_count * capacity, dtype=jnp.int32)
    picker = jnp.any(
        target.reshape(step_count * row_count, top_count)[None, :, :]
        == buffer_ids[:, None, None],
        axis=2,
    ).astype(jnp.bfloat16)
    weights = gains * live_mask[:, :, None].astype(jnp.float32)
    return (live_mask, target, picker, weights)


def shards(
    hidden_rows,
    draft_len,
    expert_ids,
    replica,
    route_gain,
    slot_up,
    slot_down,
    shared_up,
    shared_down,
):
    slot_count = lax.axis_size("expert")
    chips_x = lax.axis_size("tx")
    cores = lax.axis_size("tc")
    tensor_count = chips_x * cores
    step_count, row_count, width_part = hidden_rows.shape
    top_count = expert_ids.shape[2]
    capacity = row_count * top_count // (slot_count - slot_count // 8) + 2
    live_mask, target, picker, weights = route_plan(
        draft_len, expert_ids, replica, route_gain, slot_count, capacity
    )
    hidden_units = slot_up.shape[2]
    down_parts = jnp.concatenate([slot_down[0], shared_down], axis=0)
    down_parts = down_parts.reshape(-1, tensor_count, width_part).transpose(1, 0, 2)
    down_cols = lax.all_to_all(down_parts, TENSOR, split_axis=0, concat_axis=0, tiled=True)
    batch = jnp.dot(
        picker,
        hidden_rows.reshape(step_count * row_count, width_part),
        preferred_element_type=jnp.float32,
    ).astype(jnp.bfloat16).reshape(slot_count, step_count * capacity, width_part)
    received = lax.all_to_all(batch, "expert", split_axis=0, concat_axis=0, tiled=True)
    served = received.shape[0] * received.shape[1]
    own = step_count * row_count
    rows_part = jnp.concatenate(
        [received.reshape(served, width_part), hidden_rows.reshape(own, width_part)], axis=0
    )
    rows_x = lax.all_gather(rows_part, "tx", axis=0, tiled=False)
    rows_sibling = lax.ppermute(rows_x, "tc", [(0, 1), (1, 0)])
    core = lax.axis_index("tc")
    up_w = jnp.concatenate([slot_up[0], shared_up], axis=1).reshape(chips_x, cores, width_part, -1)
    up_own = lax.dynamic_index_in_dim(up_w, core, 1, keepdims=False)
    up_sibling = lax.dynamic_index_in_dim(up_w, 1 - core, 1, keepdims=False)
    up_value = jnp.einsum(
        "xmc,xch->mh", rows_x, up_own, preferred_element_type=jnp.float32
    ) + jnp.einsum("xmc,xch->mh", rows_sibling, up_sibling, preferred_element_type=jnp.float32)
    act = jax.nn.silu(up_value).astype(jnp.bfloat16)
    is_routed = (jnp.arange(served + own) < served)[:, None]
    act_own = jnp.where(is_routed, act[:, :hidden_units], act[:, hidden_units:])
    act_all = lax.all_gather(act_own, TENSOR, axis=0, tiled=False)
    routed_back = jnp.einsum(
        "imu,iuc->mc",
        act_all[:, :served],
        down_cols[:, :hidden_units],
        preferred_element_type=jnp.float32,
    ).astype(jnp.bfloat16).reshape(received.shape)
    shared_own = jnp.einsum(
        "imu,iuc->mc",
        act_all[:, served:],
        down_cols[:, hidden_units:],
        preferred_element_type=jnp.float32,
    ).reshape(step_count, row_count, width_part)
    answer = lax.all_to_all(routed_back, "expert", split_axis=0, concat_axis=0, tiled=True)
    slot_rows = answer.reshape(-1, width_part)
    fetched = jnp.take(slot_rows, jnp.maximum(target, 0).reshape(-1), axis=0).astype(jnp.float32)
    fetched = fetched.reshape(step_count, row_count, top_count, width_part)
    routed = jnp.sum(fetched * weights[:, :, :, None], axis=2)
    live = live_mask.astype(jnp.float32)[:, :, None]
    return ((routed + shared_own) * live).astype(jnp.bfloat16)


def solution(mesh):
    expert_count, tensor_count = mesh.devices.shape
    chip_mesh = Mesh(mesh.devices.reshape(expert_count, tensor_count // 2, 2), ("expert",) + TENSOR)
    return jax.shard_map(
        shards,
        mesh=chip_mesh,
        in_specs=(
            P(None, "expert", TENSOR),
            P(None, "expert"),
            P(None, "expert", None),
            P(None, "expert", None),
            P(None, "expert", None),
            P("expert", None, TENSOR),
            P("expert", TENSOR, None),
            P(None, TENSOR),
            P(TENSOR, None),
        ),
        out_specs=P(None, "expert", TENSOR),
        check_vma=False,
    )
```

```python
import jax
import jax.numpy as jnp
from jax import lax
from jax.sharding import PartitionSpec as P


def route_plan(lengths, chosen, second, gains, slot_count, capacity):
    step_count, row_count, top_count = chosen.shape
    span_rows = row_count // lengths.shape[1]
    positions = jnp.arange(row_count, dtype=jnp.int32)
    limit = jnp.repeat(lengths, span_rows, axis=1, total_repeat_length=row_count)
    live_mask = positions[None, :] % span_rows < limit
    replicas = slot_count // 8
    experts_all = slot_count - replicas
    slot_index = jnp.where(
        (chosen < replicas) & (second == 1), chosen + experts_all, chosen
    ).reshape(step_count, -1)
    valid = jnp.broadcast_to(live_mask[:, :, None], chosen.shape).reshape(step_count, -1)
    onehot = (
        (slot_index[:, :, None] == jnp.arange(slot_count, dtype=jnp.int32)[None, None, :])
        & valid[:, :, None]
    ).astype(jnp.int32)
    earlier = jnp.cumsum(onehot, axis=1) - onehot
    order_rank = jnp.sum(earlier * onehot, axis=2)
    step_ids = jnp.arange(step_count, dtype=jnp.int32)[:, None]
    place = (slot_index * step_count + step_ids) * capacity + order_rank
    target = jnp.where(valid, place, -1).reshape(step_count, row_count, top_count)
    buffer_ids = jnp.arange(slot_count * step_count * capacity, dtype=jnp.int32)
    picker = jnp.any(
        target.reshape(step_count * row_count, top_count)[None, :, :]
        == buffer_ids[:, None, None],
        axis=2,
    ).astype(jnp.bfloat16)
    weights = gains * live_mask[:, :, None].astype(jnp.float32)
    return (live_mask, target, picker, weights)


def shards(
    hidden_rows,
    draft_len,
    expert_ids,
    replica,
    route_gain,
    slot_up,
    slot_down,
    shared_up,
    shared_down,
):
    slot_count = lax.axis_size("expert")
    tensor_count = lax.axis_size("tensor")
    step_count, row_count, width_part = hidden_rows.shape
    top_count = expert_ids.shape[2]
    capacity = row_count * top_count // (slot_count - slot_count // 8) + 2
    live_mask, target, picker, weights = route_plan(
        draft_len, expert_ids, replica, route_gain, slot_count, capacity
    )
    hidden_units = slot_up.shape[2]
    down_parts = jnp.concatenate([slot_down[0], shared_down], axis=0)
    down_cols = lax.all_to_all(down_parts, "tensor", split_axis=1, concat_axis=0, tiled=True)
    down_cols = down_cols.reshape(tensor_count, -1, width_part)
    batch = jnp.dot(
        picker,
        hidden_rows.reshape(step_count * row_count, width_part),
        preferred_element_type=jnp.float32,
    ).astype(jnp.bfloat16).reshape(slot_count, step_count * capacity, width_part)
    received = lax.all_to_all(batch, "expert", split_axis=0, concat_axis=0, tiled=True)
    served = received.shape[0] * received.shape[1]
    own = step_count * row_count
    rows_part = jnp.concatenate(
        [received.reshape(served, width_part), hidden_rows.reshape(own, width_part)], axis=0
    )
    rows_all = lax.all_gather(rows_part, "tensor", axis=0, tiled=False)
    up_w = jnp.concatenate([slot_up[0], shared_up], axis=1).reshape(tensor_count, width_part, -1)
    up_value = jnp.einsum("tmc,tch->mh", rows_all, up_w, preferred_element_type=jnp.float32)
    act = jax.nn.silu(up_value).astype(jnp.bfloat16)
    is_routed = (jnp.arange(served + own) < served)[:, None]
    act_own = jnp.where(is_routed, act[:, :hidden_units], act[:, hidden_units:])
    act_all = lax.all_gather(act_own, "tensor", axis=0, tiled=False)
    routed_back = jnp.einsum(
        "imu,iuc->mc",
        act_all[:, :served],
        down_cols[:, :hidden_units],
        preferred_element_type=jnp.float32,
    ).astype(jnp.bfloat16).reshape(received.shape)
    shared_own = jnp.einsum(
        "imu,iuc->mc",
        act_all[:, served:],
        down_cols[:, hidden_units:],
        preferred_element_type=jnp.float32,
    ).reshape(step_count, row_count, width_part)
    answer = lax.all_to_all(routed_back, "expert", split_axis=0, concat_axis=0, tiled=True)
    slot_rows = answer.reshape(-1, width_part)
    fetched = jnp.take(slot_rows, jnp.maximum(target, 0).reshape(-1), axis=0).astype(jnp.float32)
    fetched = fetched.reshape(step_count, row_count, top_count, width_part)
    routed = jnp.sum(fetched * weights[:, :, :, None], axis=2)
    live = live_mask.astype(jnp.float32)[:, :, None]
    return ((routed + shared_own) * live).astype(jnp.bfloat16)


def solution(mesh):
    return jax.shard_map(
        shards,
        mesh=mesh,
        in_specs=(
            P(None, "expert", "tensor"),
            P(None, "expert"),
            P(None, "expert", None),
            P(None, "expert", None),
            P(None, "expert", None),
            P("expert", None, "tensor"),
            P("expert", "tensor", None),
            P(None, "tensor"),
            P("tensor", None),
        ),
        out_specs=P(None, "expert", "tensor"),
        check_vma=False,
    )
```

```python
import jax
import jax.numpy as jnp
from jax import lax
from jax.sharding import PartitionSpec as P


def route_plan(lengths, chosen, second, gains, slot_count, capacity):
    step_count, row_count, top_count = chosen.shape
    span_rows = row_count // lengths.shape[1]
    positions = jnp.arange(row_count, dtype=jnp.int32)
    limit = jnp.repeat(lengths, span_rows, axis=1, total_repeat_length=row_count)
    live_mask = positions[None, :] % span_rows < limit
    replicas = slot_count // 8
    experts_all = slot_count - replicas
    slot_index = jnp.where(
        (chosen < replicas) & (second == 1), chosen + experts_all, chosen
    ).reshape(step_count, -1)
    valid = jnp.broadcast_to(live_mask[:, :, None], chosen.shape).reshape(step_count, -1)
    onehot = (
        (slot_index[:, :, None] == jnp.arange(slot_count, dtype=jnp.int32)[None, None, :])
        & valid[:, :, None]
    ).astype(jnp.int32)
    earlier = jnp.cumsum(onehot, axis=1) - onehot
    order_rank = jnp.sum(earlier * onehot, axis=2)
    step_ids = jnp.arange(step_count, dtype=jnp.int32)[:, None]
    place = (slot_index * step_count + step_ids) * capacity + order_rank
    target = jnp.where(valid, place, -1).reshape(step_count, row_count, top_count)
    buffer_ids = jnp.arange(slot_count * step_count * capacity, dtype=jnp.int32)
    picker = jnp.any(
        target.reshape(step_count * row_count, top_count)[None, :, :]
        == buffer_ids[:, None, None],
        axis=2,
    ).astype(jnp.bfloat16)
    weights = gains * live_mask[:, :, None].astype(jnp.float32)
    return (live_mask, target, picker, weights)


def layer(
    hidden_rows,
    draft_len,
    expert_ids,
    replica,
    route_gain,
    slot_up,
    slot_down,
    shared_up,
    shared_down,
):
    slot_count = lax.axis_size("expert")
    tensor_count = lax.axis_size("tensor")
    step_count, row_count, width_part = hidden_rows.shape
    top_count = expert_ids.shape[2]
    capacity = row_count * top_count // (slot_count - slot_count // 8) + 2
    live_mask, target, picker, weights = route_plan(
        draft_len, expert_ids, replica, route_gain, slot_count, capacity
    )
    hidden_units = slot_up.shape[2]
    down_parts = jnp.concatenate([slot_down[0], shared_down], axis=0)
    down_cols = lax.all_to_all(down_parts, "tensor", split_axis=1, concat_axis=0, tiled=True)
    down_cols = down_cols.reshape(tensor_count, -1, width_part)
    batch = jnp.dot(
        picker,
        hidden_rows.reshape(step_count * row_count, width_part),
        preferred_element_type=jnp.float32,
    ).astype(jnp.bfloat16).reshape(slot_count, step_count * capacity, width_part)
    received = lax.all_to_all(batch, "expert", split_axis=0, concat_axis=0, tiled=True)
    served = received.shape[0] * received.shape[1]
    own = step_count * row_count
    rows_part = jnp.concatenate(
        [received.reshape(served, width_part), hidden_rows.reshape(own, width_part)], axis=0
    )
    rows_all = lax.all_gather(rows_part, "tensor", axis=0, tiled=False)
    up_w = jnp.concatenate([slot_up[0], shared_up], axis=1).reshape(tensor_count, width_part, -1)
    up_w = lax.optimization_barrier(up_w)
    up_value = jnp.einsum("tmc,tch->mh", rows_all, up_w, preferred_element_type=jnp.float32)
    act = jax.nn.silu(up_value).astype(jnp.bfloat16)
    is_routed = (jnp.arange(served + own) < served)[:, None]
    act_own = jnp.where(is_routed, act[:, :hidden_units], act[:, hidden_units:])
    act_all = lax.all_gather(act_own, "tensor", axis=0, tiled=False)
    routed_back = jnp.einsum(
        "imu,iuc->mc",
        act_all[:, :served],
        down_cols[:, :hidden_units],
        preferred_element_type=jnp.float32,
    ).astype(jnp.bfloat16).reshape(received.shape)
    shared_own = jnp.einsum(
        "imu,iuc->mc",
        act_all[:, served:],
        down_cols[:, hidden_units:],
        preferred_element_type=jnp.float32,
    ).reshape(step_count, row_count, width_part)
    answer = lax.all_to_all(routed_back, "expert", split_axis=0, concat_axis=0, tiled=True)
    slot_rows = answer.reshape(-1, width_part)
    fetched = jnp.take(slot_rows, jnp.maximum(target, 0).reshape(-1), axis=0).astype(jnp.float32)
    fetched = fetched.reshape(step_count, row_count, top_count, width_part)
    routed = jnp.sum(fetched * weights[:, :, :, None], axis=2)
    live = live_mask.astype(jnp.float32)[:, :, None]
    return ((routed + shared_own) * live).astype(jnp.bfloat16)


def solution(mesh):
    return jax.shard_map(
        layer,
        mesh=mesh,
        in_specs=(
            P(None, "expert", "tensor"),
            P(None, "expert"),
            P(None, "expert", None),
            P(None, "expert", None),
            P(None, "expert", None),
            P("expert", None, "tensor"),
            P("expert", "tensor", None),
            P(None, "tensor"),
            P("tensor", None),
        ),
        out_specs=P(None, "expert", "tensor"),
        check_vma=False,
    )
```

```python
import jax
import jax.numpy as jnp
from jax import lax
from jax.sharding import PartitionSpec as P


def route_plan(lengths, chosen, second, gains, slot_count, capacity):
    step_count, row_count, top_count = chosen.shape
    span_rows = row_count // lengths.shape[1]
    positions = jnp.arange(row_count, dtype=jnp.int32)
    limit = jnp.repeat(lengths, span_rows, axis=1, total_repeat_length=row_count)
    live_mask = positions[None, :] % span_rows < limit
    replicas = slot_count // 8
    experts_all = slot_count - replicas
    slot_index = jnp.where(
        (chosen < replicas) & (second == 1), chosen + experts_all, chosen
    ).reshape(step_count, -1)
    valid = jnp.broadcast_to(live_mask[:, :, None], chosen.shape).reshape(step_count, -1)
    onehot = (
        (slot_index[:, :, None] == jnp.arange(slot_count, dtype=jnp.int32)[None, None, :])
        & valid[:, :, None]
    ).astype(jnp.int32)
    earlier = jnp.cumsum(onehot, axis=1) - onehot
    order_rank = jnp.sum(earlier * onehot, axis=2)
    step_ids = jnp.arange(step_count, dtype=jnp.int32)[:, None]
    place = (slot_index * step_count + step_ids) * capacity + order_rank
    target = jnp.where(valid, place, -1).reshape(step_count, row_count, top_count)
    buffer_ids = jnp.arange(slot_count * step_count * capacity, dtype=jnp.int32)
    picker = jnp.any(
        target.reshape(step_count * row_count, top_count)[None, :, :]
        == buffer_ids[:, None, None],
        axis=2,
    ).astype(jnp.bfloat16)
    weights = gains * live_mask[:, :, None].astype(jnp.float32)
    return (live_mask, target, picker, weights)


def layer(
    hidden_rows,
    draft_len,
    expert_ids,
    replica,
    route_gain,
    slot_up,
    slot_down,
    shared_up,
    shared_down,
):
    slot_count = lax.axis_size("expert")
    tensor_count = lax.axis_size("tensor")
    step_count, row_count, width_part = hidden_rows.shape
    top_count = expert_ids.shape[2]
    capacity = row_count * top_count // (slot_count - slot_count // 8) + 2
    live_mask, target, picker, weights = route_plan(
        draft_len, expert_ids, replica, route_gain, slot_count, capacity
    )
    hidden_units = slot_up.shape[2]
    down_parts = jnp.concatenate([slot_down[0], shared_down], axis=0)
    down_cols = lax.all_to_all(down_parts, "tensor", split_axis=1, concat_axis=0, tiled=True)
    down_cols = down_cols.reshape(tensor_count, -1, width_part)
    batch = jnp.dot(
        picker,
        hidden_rows.reshape(step_count * row_count, width_part),
        preferred_element_type=jnp.float32,
    ).astype(jnp.bfloat16).reshape(slot_count, step_count * capacity, width_part)
    received = lax.all_to_all(batch, "expert", split_axis=0, concat_axis=0, tiled=True)
    served = received.shape[0] * received.shape[1]
    own = step_count * row_count
    served_all, own_all = lax.all_gather(
        (received.reshape(served, width_part), hidden_rows.reshape(own, width_part)),
        "tensor",
        axis=0,
        tiled=False,
    )
    up_w = slot_up[0].reshape(tensor_count, width_part, -1)
    shared_w = shared_up.reshape(tensor_count, width_part, -1)
    act_served = jax.nn.silu(
        jnp.einsum("tmc,tch->mh", served_all, up_w, preferred_element_type=jnp.float32)
    ).astype(jnp.bfloat16)
    act_shared = jax.nn.silu(
        jnp.einsum("tmc,tch->mh", own_all, shared_w, preferred_element_type=jnp.float32)
    ).astype(jnp.bfloat16)
    act_own = jnp.concatenate([act_served, act_shared], axis=0)
    act_all = lax.all_gather(act_own, "tensor", axis=0, tiled=False)
    routed_back = jnp.einsum(
        "imu,iuc->mc",
        act_all[:, :served],
        down_cols[:, :hidden_units],
        preferred_element_type=jnp.float32,
    ).astype(jnp.bfloat16).reshape(received.shape)
    shared_own = jnp.einsum(
        "imu,iuc->mc",
        act_all[:, served:],
        down_cols[:, hidden_units:],
        preferred_element_type=jnp.float32,
    ).reshape(step_count, row_count, width_part)
    answer = lax.all_to_all(routed_back, "expert", split_axis=0, concat_axis=0, tiled=True)
    slot_rows = answer.reshape(-1, width_part)
    fetched = jnp.take(slot_rows, jnp.maximum(target, 0).reshape(-1), axis=0).astype(jnp.float32)
    fetched = fetched.reshape(step_count, row_count, top_count, width_part)
    routed = jnp.sum(fetched * weights[:, :, :, None], axis=2)
    live = live_mask.astype(jnp.float32)[:, :, None]
    return ((routed + shared_own) * live).astype(jnp.bfloat16)


def solution(mesh):
    return jax.shard_map(
        layer,
        mesh=mesh,
        in_specs=(
            P(None, "expert", "tensor"),
            P(None, "expert"),
            P(None, "expert", None),
            P(None, "expert", None),
            P(None, "expert", None),
            P("expert", None, "tensor"),
            P("expert", "tensor", None),
            P(None, "tensor"),
            P("tensor", None),
        ),
        out_specs=P(None, "expert", "tensor"),
        check_vma=False,
    )
```

```python
import jax
import jax.numpy as jnp
from jax import lax
from jax.sharding import PartitionSpec as P


def route_plan(lengths, chosen, second, gains, slot_count, capacity):
    step_count, row_count, top_count = chosen.shape
    span_rows = row_count // lengths.shape[1]
    positions = jnp.arange(row_count, dtype=jnp.int32)
    limit = jnp.repeat(lengths, span_rows, axis=1, total_repeat_length=row_count)
    live_mask = positions[None, :] % span_rows < limit
    replicas = slot_count // 8
    experts_all = slot_count - replicas
    slot_index = jnp.where(
        (chosen < replicas) & (second == 1), chosen + experts_all, chosen
    ).reshape(step_count, -1)
    valid = jnp.broadcast_to(live_mask[:, :, None], chosen.shape).reshape(step_count, -1)
    onehot = (
        (slot_index[:, :, None] == jnp.arange(slot_count, dtype=jnp.int32)[None, None, :])
        & valid[:, :, None]
    ).astype(jnp.int32)
    earlier = jnp.cumsum(onehot, axis=1) - onehot
    order_rank = jnp.sum(earlier * onehot, axis=2)
    step_ids = jnp.arange(step_count, dtype=jnp.int32)[:, None]
    place = (slot_index * step_count + step_ids) * capacity + order_rank
    target = jnp.where(valid, place, -1).reshape(step_count, row_count, top_count)
    buffer_ids = jnp.arange(slot_count * step_count * capacity, dtype=jnp.int32)
    picker = jnp.any(
        target.reshape(step_count * row_count, top_count)[None, :, :]
        == buffer_ids[:, None, None],
        axis=2,
    ).astype(jnp.bfloat16)
    weights = gains * live_mask[:, :, None].astype(jnp.float32)
    return (live_mask, target, picker, weights)


def layer(
    hidden_rows,
    draft_len,
    expert_ids,
    replica,
    route_gain,
    slot_up,
    slot_down,
    shared_up,
    shared_down,
):
    slot_count = lax.axis_size("expert")
    tensor_count = lax.axis_size("tensor")
    step_count, row_count, width_part = hidden_rows.shape
    top_count = expert_ids.shape[2]
    capacity = row_count * top_count // (slot_count - slot_count // 8) + 2
    live_mask, target, picker, weights = route_plan(
        draft_len, expert_ids, replica, route_gain, slot_count, capacity
    )
    hidden_units = slot_up.shape[2]
    down_parts = jnp.concatenate([slot_down[0], shared_down], axis=0)
    down_cols = lax.all_to_all(down_parts, "tensor", split_axis=1, concat_axis=0, tiled=True)
    down_cols = down_cols.reshape(tensor_count, -1, width_part)
    batch = jnp.dot(
        picker,
        hidden_rows.reshape(step_count * row_count, width_part),
        preferred_element_type=jnp.float32,
    ).astype(jnp.bfloat16).reshape(slot_count, step_count * capacity, width_part)
    received = lax.all_to_all(batch, "expert", split_axis=0, concat_axis=0, tiled=True)
    served = received.shape[0] * received.shape[1]
    own = step_count * row_count
    served_all, own_all = lax.all_gather(
        (received.reshape(served, width_part), hidden_rows.reshape(own, width_part)),
        "tensor",
        axis=0,
        tiled=False,
    )
    up_w = slot_up[0].reshape(tensor_count, width_part, -1)
    shared_w = shared_up.reshape(tensor_count, width_part, -1)
    act_served = jax.nn.silu(
        jnp.einsum("tmc,tch->mh", served_all, up_w, preferred_element_type=jnp.float32)
    ).astype(jnp.bfloat16)
    act_shared = jax.nn.silu(
        jnp.einsum("tmc,tch->mh", own_all, shared_w, preferred_element_type=jnp.float32)
    ).astype(jnp.bfloat16)
    act_served_all, act_shared_all = lax.all_gather(
        (act_served, act_shared), "tensor", axis=0, tiled=False
    )
    routed_back = jnp.einsum(
        "imu,iuc->mc",
        act_served_all,
        down_cols[:, :hidden_units],
        preferred_element_type=jnp.float32,
    ).astype(jnp.bfloat16).reshape(received.shape)
    shared_own = jnp.einsum(
        "imu,iuc->mc",
        act_shared_all,
        down_cols[:, hidden_units:],
        preferred_element_type=jnp.float32,
    ).reshape(step_count, row_count, width_part)
    answer = lax.all_to_all(routed_back, "expert", split_axis=0, concat_axis=0, tiled=True)
    slot_rows = answer.reshape(-1, width_part)
    fetched = jnp.take(slot_rows, jnp.maximum(target, 0).reshape(-1), axis=0).astype(jnp.float32)
    fetched = fetched.reshape(step_count, row_count, top_count, width_part)
    routed = jnp.sum(fetched * weights[:, :, :, None], axis=2)
    live = live_mask.astype(jnp.float32)[:, :, None]
    return ((routed + shared_own) * live).astype(jnp.bfloat16)


def solution(mesh):
    return jax.shard_map(
        layer,
        mesh=mesh,
        in_specs=(
            P(None, "expert", "tensor"),
            P(None, "expert"),
            P(None, "expert", None),
            P(None, "expert", None),
            P(None, "expert", None),
            P("expert", None, "tensor"),
            P("expert", "tensor", None),
            P(None, "tensor"),
            P("tensor", None),
        ),
        out_specs=P(None, "expert", "tensor"),
        check_vma=False,
    )
```
